512 devices in a mesh: lat: 32 (over z, x), lon: 16 (over y, core).
Axes of the slice: x: 4, y: 8, z: 8, core: 2. Of those that a mesh axis runs over, the one named last changes fastest.
Arguments:
- grid: bfloat16 [144, 128, 5136], P(None, 'lat', 'lon'), may hold values from -6 to 6
- cubic_weights: float32 [4, 128, 5136], P(None, 'lat', 'lon'), as said below
- dep_base: int32 [128, 5136], P('lat', 'lon'), may hold values from -2 to 128, as said below
- row_points: int32 [128], P('lat'), may hold values from 20 to 5136, as said below
- wave_order: int32 [640], replicated, may hold values from 0 to 639, each once
- legendre: bfloat16 [640, 128, 640], P('lat'), may hold values from -24 to 24
Outputs:
- spectral: bfloat16 [640, 144, 2, 640], P('lat', 'lon')
The draws below stay inside these ranges and needn't reach their ends.
Inputs may be any that keep to these rules, and one draw needn't show every extreme that they name: dep_base[r, j] - r is one of -2, -1, 0, 1. `row_points`: every entry is 20 + 4 i for a whole number i. `cubic_weights`: the four weights of a point are the cubic Lagrange weights at nodes -1, 0, 1, 2 for one fraction in 0 to 1.
All inputs are finite; a program needn't handle non-finite values.
Results may differ from the reference program's by a relative error of at most 0.0062.
Values may be sent and summed in bfloat16 or wider, within the bound.
No kernel may reach another device: no remote copies, remote signals or barrier semaphores. Data moves between devices by JAX's collectives and lax.ppermute only.
A program may use at most 64 MiB of HBM per device.

```python
import math
import jax
import jax.numpy as jnp
from jax import lax

PTS = 5136
M = 640
NDEG = 640
HALO = 3
COLS = 144
LAT = 128
N_LON = 16


def draw_cubic_weights(key, part):
    uniform_draw = jax.random.uniform(key, (LAT, PTS), jnp.float32)
    fraction = uniform_draw
    first = -fraction * (fraction - 1.0) * (fraction - 2.0) / 6.0
    second = (fraction + 1.0) * (fraction - 1.0) * (fraction - 2.0) / 2.0
    third = -(fraction + 1.0) * fraction * (fraction - 2.0) / 2.0
    fourth = (fraction + 1.0) * fraction * (fraction - 1.0) / 6.0
    return jnp.stack([first, second, third, fourth], axis=0).astype(jnp.float32)


def draw_dep_base(key, part):
    offsets = jax.random.randint(key, (LAT, PTS), -2, 2, dtype=jnp.int32)
    offsets = offsets.at[0, 0].set(-2).at[LAT - 1, 0].set(1)
    return (jnp.arange(LAT, dtype=jnp.int32)[:, None] + offsets).astype(jnp.int32)


def draw_row_points(key, part):
    cycle = jax.random.randint(key, (LAT,), 0, (PTS - 20) // 4 + 1, dtype=jnp.int32)
    lengths = 20 + 4 * cycle
    lengths = lengths.at[0].set(PTS).at[LAT - 1].set(20)
    return lengths.astype(jnp.int32)


def steps_of(rng, extent, split, smallest, top_value):
    def one(dim, shards_of):
        draws = jax.random.uniform(jax.random.fold_in(jax.random.fold_in(rng, 6), dim), (shards_of,), jnp.float32, smallest / len(split), top_value / len(split))
        return jnp.repeat(jnp.exp(draws), extent[dim] // shards_of).reshape((-1,) + (1,) * (len(extent) - dim - 1))

    loudness = one(*split[0])
    for cut in split[1:]:
        loudness = loudness * one(*cut)
    return loudness


def gaussian(key, extent, scale, bound, shards=(), kind=jnp.bfloat16):
    entries = jax.random.normal(key, extent, jnp.float32) * scale
    if len(shards) > 0:
        entries = steps_of(key, extent, shards, -0.22, 0.18) * entries
    return jnp.clip(entries, min=-bound, max=bound).astype(kind)


def setup_inputs(seed: int = 0) -> dict:
    key_of = jax.random.split(jax.random.key(seed), 7)
    grid = gaussian(key_of[0], (COLS, LAT, PTS), 1.0, 6.0, ((1, 32), (2, 16)))
    cubic_weights = draw_cubic_weights(jax.random.fold_in(key_of[6], 71), 0)
    dep_base = draw_dep_base(jax.random.fold_in(key_of[6], 71), 0)
    row_points = draw_row_points(jax.random.fold_in(key_of[6], 71), 0)
    wave_order = jax.random.permutation(key_of[4], M).astype(jnp.int32)
    legendre = gaussian(key_of[5], (M, LAT, NDEG), 4.0, 24.0, ((0, 32),))
    return {"grid": grid, "cubic_weights": cubic_weights, "dep_base": dep_base, "row_points": row_points, "wave_order": wave_order, "legendre": legendre}


def segment_tables(points, seg_len, waves):
    wavenumber = jnp.arange(waves, dtype=jnp.int32)
    position = jnp.arange(seg_len, dtype=jnp.int32)
    product = (position[None, :, None] * wavenumber[None, None, :]) % points[:, None, None]
    angles = (2.0 * math.pi) * product.astype(jnp.float32) / points[:, None, None].astype(jnp.float32)
    return jnp.concatenate([jnp.cos(angles), -jnp.sin(angles)], axis=2).astype(jnp.bfloat16)


def phase_pair(points, starts, waves):
    wavenumber = jnp.arange(waves, dtype=jnp.int32)
    shifted = starts[None, :] % points[:, None]
    product = (shifted[:, :, None] * wavenumber[None, None, :]) % points[:, None, None]
    angles = (2.0 * math.pi) * product.astype(jnp.float32) / points[:, None, None].astype(jnp.float32)
    return jnp.cos(angles), -jnp.sin(angles)


def reference(grid, cubic_weights, dep_base, row_points, wave_order, legendre):
    pieces = N_LON
    seg_len = PTS // N_LON
    padded = jnp.pad(grid, ((0, 0), (HALO, HALO), (0, 0)))
    row_ids = jnp.arange(LAT, dtype=jnp.int32)
    offset = dep_base - row_ids[:, None]
    weights_rows = jnp.transpose(cubic_weights, (1, 0, 2))
    starts = jnp.arange(pieces, dtype=jnp.int32) * seg_len
    wavenumber = jnp.arange(M, dtype=jnp.int32)
    points_index = jnp.arange(PTS, dtype=jnp.int32)

    def one_row(inputs):
        row, points, row_offset, row_weights = inputs
        window = lax.dynamic_slice(padded, (jnp.int32(0), row.astype(jnp.int32), jnp.int32(0)), (COLS, 2 * HALO + 1, PTS))
        arrival = jnp.zeros((COLS, PTS), jnp.float32)
        for displace in range(-HALO, HALO + 1):
            stencil = jnp.zeros((PTS,), jnp.float32)
            for node in range(4):
                stencil = stencil + jnp.where(row_offset - 1 + node == displace, row_weights[node], jnp.float32(0.0))
            arrival = arrival + stencil[None, :] * window[:, HALO + displace, :].astype(jnp.float32)
        arrival = jnp.where(points_index[None, :] < points, arrival, jnp.float32(0.0)).astype(jnp.bfloat16)
        tables = segment_tables(points[None], seg_len, M)[0]
        phase_re, phase_im = phase_pair(points[None], starts, M)
        pieces_rows = arrival.reshape(COLS, pieces, seg_len).astype(jnp.float32)
        spectra = jnp.einsum("cpj,jx->cpx", pieces_rows, tables.astype(jnp.float32)).reshape(COLS, pieces, 2, M)
        real_part = jnp.sum(phase_re[0][None] * spectra[:, :, 0] - phase_im[0][None] * spectra[:, :, 1], axis=1)
        imag_part = jnp.sum(phase_re[0][None] * spectra[:, :, 1] + phase_im[0][None] * spectra[:, :, 0], axis=1)
        fourier = jnp.stack([real_part, imag_part], axis=1)
        inverse = jnp.float32(1.0) / points.astype(jnp.float32)
        resolved = 2 * wavenumber < points
        fourier = jnp.where(resolved[None, None, :], fourier * inverse, jnp.float32(0.0))
        return fourier.astype(jnp.bfloat16)

    by_rows = lax.map(one_row, (row_ids, row_points, offset, weights_rows))
    fourier = jnp.transpose(by_rows, (1, 0, 2, 3))
    sorted_waves = jnp.take(fourier, wave_order, axis=3).astype(jnp.float32)
    degree = jnp.arange(NDEG, dtype=jnp.int32)
    masked_table = jnp.where(degree[None, None, :] >= wave_order[:, None, None], legendre, jnp.zeros((), legendre.dtype))
    spectral = jnp.einsum("clts,sln->sctn", sorted_waves, masked_table.astype(jnp.float32))
    return spectral.astype(jnp.bfloat16)
```

```python
import math

import jax
import jax.numpy as jnp
from jax import lax
from jax.sharding import PartitionSpec as P

M = 640
NDEG = 640
HALO = 3
SPLIT = 64


def extended(block, sides, width):
    for axis, dim in sides:
        count = lax.axis_size(axis)
        forward = [(i, i + 1) for i in range(count - 1)]
        backward = [(target, source) for source, target in forward]
        low = lax.ppermute(
            lax.slice_in_dim(block, block.shape[dim] - width, None, axis=dim), axis, forward
        )
        high = lax.ppermute(lax.slice_in_dim(block, 0, width, axis=dim), axis, backward)
        block = jnp.concatenate([low, block, high], axis=dim)
    return block


def angles_of(points, position, wavenumber):
    product = position[None, :, None] * wavenumber[None, None, :] % points[:, None, None]
    return 2.0 * math.pi * product.astype(jnp.float32) / points[:, None, None].astype(jnp.float32)


def segment_tables(points, seg_len, waves):
    position = jnp.arange(seg_len, dtype=jnp.int32)
    high = angles_of(points, position, jnp.arange(waves // SPLIT, dtype=jnp.int32) * SPLIT)
    low = angles_of(points, position, jnp.arange(SPLIT, dtype=jnp.int32))
    ch, sh = jnp.cos(high)[..., :, None], jnp.sin(high)[..., :, None]
    cl, sl = jnp.cos(low)[..., None, :], jnp.sin(low)[..., None, :]
    shape = (points.shape[0], seg_len, waves)
    cosine = (ch * cl - sh * sl).reshape(shape)
    sine = (sh * cl + ch * sl).reshape(shape)
    return jnp.stack([cosine, -sine], axis=2).astype(jnp.bfloat16)


def phase_pair(points, starts, waves):
    wavenumber = jnp.arange(waves, dtype=jnp.int32)
    shifted = starts[None, :] % points[:, None]
    product = shifted[:, :, None] * wavenumber[None, None, :] % points[:, None, None]
    angles = 2.0 * math.pi * product.astype(jnp.float32) / points[:, None, None].astype(jnp.float32)
    return (jnp.cos(angles), -jnp.sin(angles))


def shards(grid, cubic_weights, dep_base, row_points, wave_order, legendre):
    columns, band_rows, seg_len = grid.shape
    pieces = lax.axis_size("lon")
    keep = columns // pieces
    slots = legendre.shape[0]
    first_row = lax.axis_index("lat") * band_rows
    first_point = lax.axis_index("lon") * seg_len
    padded = extended(grid, (("lat", 1),), HALO)
    offset = dep_base - (first_row + jnp.arange(band_rows, dtype=jnp.int32))[:, None]
    arrival = jnp.zeros((columns, band_rows, seg_len), jnp.float32)
    for displace in range(-HALO, HALO + 1):
        stencil = jnp.zeros((band_rows, seg_len), jnp.float32)
        for node in range(4):
            stencil = stencil + jnp.where(
                offset - 1 + node == displace, cubic_weights[node], jnp.float32(0.0)
            )
        arrival = arrival + stencil[None] * padded[
            :, HALO + displace : HALO + displace + band_rows, :
        ].astype(jnp.float32)
    inside = (first_point + jnp.arange(seg_len, dtype=jnp.int32))[None, :] < row_points[:, None]
    arrival = jnp.where(inside[None], arrival, jnp.float32(0.0)).astype(jnp.bfloat16)
    gathered = lax.all_to_all(
        arrival.reshape(pieces, keep, band_rows, seg_len), "lon", split_axis=0, concat_axis=0, tiled=True
    )
    tables = segment_tables(row_points, seg_len, M)
    starts = jnp.arange(pieces, dtype=jnp.int32) * seg_len
    phase_re, phase_im = phase_pair(row_points, starts, M)
    spectra = jnp.einsum(
        "pcrj,rjtx->rtpcx", gathered, tables, preferred_element_type=jnp.float32
    )
    real_part = jnp.sum(
        phase_re[:, :, None, :] * spectra[:, 0] - phase_im[:, :, None, :] * spectra[:, 1], axis=1
    )
    imag_part = jnp.sum(
        phase_re[:, :, None, :] * spectra[:, 1] + phase_im[:, :, None, :] * spectra[:, 0], axis=1
    )
    fourier = jnp.stack([real_part, imag_part], axis=2).transpose(1, 0, 2, 3)
    wavenumber = jnp.arange(M, dtype=jnp.int32)
    inverse = jnp.float32(1.0) / row_points.astype(jnp.float32)
    resolved = 2 * wavenumber[None, :] < row_points[:, None]
    fourier = jnp.where(
        resolved[None, :, None, :], fourier * inverse[None, :, None, None], jnp.float32(0.0)
    )
    fourier = fourier.astype(jnp.bfloat16)
    sorted_waves = jnp.take(fourier, wave_order, axis=3)
    my_slots = lax.dynamic_slice_in_dim(wave_order, lax.axis_index("lat") * slots, slots)
    degree = jnp.arange(NDEG, dtype=jnp.int32)
    masked_table = jnp.where(
        degree[None, None, :] >= my_slots[:, None, None], legendre, jnp.zeros((), legendre.dtype)
    )
    result = jnp.einsum(
        "clts,sln->sctn",
        lax.all_to_all(sorted_waves, "lat", split_axis=3, concat_axis=1, tiled=True),
        masked_table,
        preferred_element_type=jnp.float32,
    )
    return result.astype(jnp.bfloat16)


def solution(mesh):
    return jax.shard_map(
        shards,
        mesh=mesh,
        in_specs=(
            P(None, "lat", "lon"),
            P(None, "lat", "lon"),
            P("lat", "lon"),
            P("lat"),
            P(),
            P("lat", None, None),
        ),
        out_specs=P("lat", "lon", None, None),
        check_vma=False,
    )
```

```python
import math

import jax
import jax.numpy as jnp
from jax import lax
from jax.sharding import PartitionSpec as P

M = 640
NDEG = 640
HALO = 3
SPLIT = 64
LAT = ("lat_outer", "lat_inner")


def extended(block, sides, width):
    for axis, dim in sides:
        count = lax.axis_size(axis)
        forward = [(i, i + 1) for i in range(count - 1)]
        backward = [(target, source) for source, target in forward]
        low = lax.ppermute(
            lax.slice_in_dim(block, block.shape[dim] - width, None, axis=dim), axis, forward
        )
        high = lax.ppermute(lax.slice_in_dim(block, 0, width, axis=dim), axis, backward)
        block = jnp.concatenate([low, block, high], axis=dim)
    return block


def angles_of(points, position, wavenumber):
    product = position[None, :, None] * wavenumber[None, None, :] % points[:, None, None]
    return 2.0 * math.pi * product.astype(jnp.float32) / points[:, None, None].astype(jnp.float32)


def segment_tables(points, seg_len, waves):
    position = jnp.arange(seg_len, dtype=jnp.int32)
    high = angles_of(points, position, jnp.arange(waves // SPLIT, dtype=jnp.int32) * SPLIT)
    low = angles_of(points, position, jnp.arange(SPLIT, dtype=jnp.int32))
    ch, sh = jnp.cos(high)[..., :, None], jnp.sin(high)[..., :, None]
    cl, sl = jnp.cos(low)[..., None, :], jnp.sin(low)[..., None, :]
    shape = (points.shape[0], seg_len, waves)
    cosine = (ch * cl - sh * sl).reshape(shape)
    sine = (sh * cl + ch * sl).reshape(shape)
    return jnp.stack([cosine, -sine], axis=2).astype(jnp.bfloat16)


def phase_pair(points, starts, waves):
    wavenumber = jnp.arange(waves, dtype=jnp.int32)
    shifted = starts[None, :] % points[:, None]
    product = shifted[:, :, None] * wavenumber[None, None, :] % points[:, None, None]
    angles = 2.0 * math.pi * product.astype(jnp.float32) / points[:, None, None].astype(jnp.float32)
    return (jnp.cos(angles), -jnp.sin(angles))


def shards(grid, cubic_weights, dep_base, row_points, wave_order, legendre):
    columns, band_rows, seg_len = grid.shape
    pieces = lax.axis_size("lon")
    keep = columns // pieces
    slots = legendre.shape[0]
    first_row = lax.axis_index(LAT) * band_rows
    first_point = lax.axis_index("lon") * seg_len
    padded = extended(grid, ((LAT, 1),), HALO)
    offset = dep_base - (first_row + jnp.arange(band_rows, dtype=jnp.int32))[:, None]
    arrival = jnp.zeros((columns, band_rows, seg_len), jnp.float32)
    for displace in range(-HALO, HALO + 1):
        stencil = jnp.zeros((band_rows, seg_len), jnp.float32)
        for node in range(4):
            stencil = stencil + jnp.where(
                offset - 1 + node == displace, cubic_weights[node], jnp.float32(0.0)
            )
        arrival = arrival + stencil[None] * padded[
            :, HALO + displace : HALO + displace + band_rows, :
        ].astype(jnp.float32)
    inside = (first_point + jnp.arange(seg_len, dtype=jnp.int32))[None, :] < row_points[:, None]
    arrival = jnp.where(inside[None], arrival, jnp.float32(0.0)).astype(jnp.bfloat16)
    gathered = lax.all_to_all(
        arrival.reshape(pieces, keep, band_rows, seg_len), "lon", split_axis=0, concat_axis=0, tiled=True
    )
    tables = segment_tables(row_points, seg_len, M)
    starts = jnp.arange(pieces, dtype=jnp.int32) * seg_len
    phase_re, phase_im = phase_pair(row_points, starts, M)
    spectra = jnp.einsum(
        "pcrj,rjtx->rtpcx", gathered, tables, preferred_element_type=jnp.float32
    )
    real_part = jnp.sum(
        phase_re[:, :, None, :] * spectra[:, 0] - phase_im[:, :, None, :] * spectra[:, 1], axis=1
    )
    imag_part = jnp.sum(
        phase_re[:, :, None, :] * spectra[:, 1] + phase_im[:, :, None, :] * spectra[:, 0], axis=1
    )
    fourier = jnp.stack([real_part, imag_part], axis=2)
    wavenumber = jnp.arange(M, dtype=jnp.int32)
    inverse = jnp.float32(1.0) / row_points.astype(jnp.float32)
    resolved = 2 * wavenumber[None, :] < row_points[:, None]
    fourier = jnp.where(
        resolved[:, None, None, :], fourier * inverse[:, None, None, None], jnp.float32(0.0)
    )
    fourier = fourier.astype(jnp.bfloat16)
    pick = (wave_order[None, :] == wavenumber[:, None]).astype(jnp.bfloat16)
    sorted_waves = jnp.einsum(
        "rctm,ms->sctr", fourier, pick, preferred_element_type=jnp.float32
    ).astype(jnp.bfloat16)
    outer, inner = lax.axis_size(LAT[0]), lax.axis_size(LAT[1])
    sorted_waves = sorted_waves.reshape((outer, inner, slots) + sorted_waves.shape[1:])
    sorted_waves = lax.all_to_all(sorted_waves, LAT[1], split_axis=1, concat_axis=1, tiled=True)
    sorted_waves = lax.all_to_all(sorted_waves, LAT[0], split_axis=0, concat_axis=0, tiled=True)
    sorted_waves = sorted_waves.reshape((outer * inner,) + sorted_waves.shape[2:])
    my_slots = lax.dynamic_slice_in_dim(wave_order, lax.axis_index(LAT) * slots, slots)
    degree = jnp.arange(NDEG, dtype=jnp.int32)
    masked_table = jnp.where(
        degree[None, None, :] >= my_slots[:, None, None], legendre, jnp.zeros((), legendre.dtype)
    )
    masked_table = masked_table.reshape(slots, outer * inner, band_rows, NDEG)
    result = jnp.einsum(
        "qsctr,sqrn->sctn", sorted_waves, masked_table, preferred_element_type=jnp.float32
    )
    return result.astype(jnp.bfloat16)


def lat_split(mesh):
    count = mesh.shape["lat"]
    fast = len({tuple(getattr(d, "coords", (0,)))[0] for d in mesh.devices[:, 0]})
    if fast < 1 or count % fast != 0:
        fast = 1
    return count // fast, fast


def solution(mesh):
    outer, inner = lat_split(mesh)
    grid_mesh = jax.sharding.Mesh(
        mesh.devices.reshape(outer, inner, mesh.shape["lon"]), LAT + ("lon",)
    )
    return jax.shard_map(
        shards,
        mesh=grid_mesh,
        in_specs=(
            P(None, LAT, "lon"),
            P(None, LAT, "lon"),
            P(LAT, "lon"),
            P(LAT),
            P(),
            P(LAT, None, None),
        ),
        out_specs=P(LAT, "lon", None, None),
        check_vma=False,
    )
```

```python
import math

import jax
import jax.numpy as jnp
from jax import lax
from jax.sharding import PartitionSpec as P

M = 640
NDEG = 640
HALO = 3
SPLIT = 32
LAT = ("lat_outer", "lat_inner")


def extended(block, sides, width):
    for axis, dim in sides:
        count = lax.axis_size(axis)
        forward = [(i, i + 1) for i in range(count - 1)]
        backward = [(target, source) for source, target in forward]
        low = lax.ppermute(
            lax.slice_in_dim(block, block.shape[dim] - width, None, axis=dim), axis, forward
        )
        high = lax.ppermute(lax.slice_in_dim(block, 0, width, axis=dim), axis, backward)
        block = jnp.concatenate([low, block, high], axis=dim)
    return block


def angles_of(points, position, wavenumber):
    product = position[None, :, None] * wavenumber[None, None, :] % points[:, None, None]
    return 2.0 * math.pi * product.astype(jnp.float32) / points[:, None, None].astype(jnp.float32)


def segment_tables(points, seg_len, waves):
    wavenumber = jnp.arange(waves, dtype=jnp.int32)
    high = angles_of(points, jnp.arange(-(-seg_len // SPLIT), dtype=jnp.int32) * SPLIT, wavenumber)
    low = angles_of(points, jnp.arange(SPLIT, dtype=jnp.int32), wavenumber)
    ch, sh = jnp.cos(high)[:, :, None, :], jnp.sin(high)[:, :, None, :]
    cl, sl = jnp.cos(low)[:, None, :, :], jnp.sin(low)[:, None, :, :]
    cosine = ch * cl - sh * sl
    sine = sh * cl + ch * sl
    table = jnp.concatenate([cosine, -sine], axis=3).astype(jnp.bfloat16)
    return table.reshape(points.shape[0], -1, 2 * waves)[:, :seg_len]


def phase_pair(points, starts, waves):
    wavenumber = jnp.arange(waves, dtype=jnp.int32)
    shifted = starts[None, :] % points[:, None]
    product = shifted[:, :, None] * wavenumber[None, None, :] % points[:, None, None]
    angles = 2.0 * math.pi * product.astype(jnp.float32) / points[:, None, None].astype(jnp.float32)
    return (jnp.cos(angles), -jnp.sin(angles))


def shards(grid, cubic_weights, dep_base, row_points, wave_order, legendre):
    columns, band_rows, seg_len = grid.shape
    pieces = lax.axis_size("lon")
    keep = columns // pieces
    slots = legendre.shape[0]
    first_row = lax.axis_index(LAT) * band_rows
    first_point = lax.axis_index("lon") * seg_len
    padded = extended(grid, ((LAT, 1),), HALO)
    offset = dep_base - (first_row + jnp.arange(band_rows, dtype=jnp.int32))[:, None]
    arrival = jnp.zeros((columns, band_rows, seg_len), jnp.float32)
    for displace in range(-HALO, HALO + 1):
        stencil = jnp.zeros((band_rows, seg_len), jnp.float32)
        for node in range(4):
            stencil = stencil + jnp.where(
                offset - 1 + node == displace, cubic_weights[node], jnp.float32(0.0)
            )
        arrival = arrival + stencil[None] * padded[
            :, HALO + displace : HALO + displace + band_rows, :
        ].astype(jnp.float32)
    inside = (first_point + jnp.arange(seg_len, dtype=jnp.int32))[None, :] < row_points[:, None]
    arrival = jnp.where(inside[None], arrival, jnp.float32(0.0)).astype(jnp.bfloat16)
    gathered = lax.all_to_all(
        arrival.reshape(pieces, keep, band_rows, seg_len), "lon", split_axis=0, concat_axis=0, tiled=True
    )
    tables = segment_tables(row_points, seg_len, M)
    starts = jnp.arange(pieces, dtype=jnp.int32) * seg_len
    phase_re, phase_im = phase_pair(row_points, starts, M)
    spectra = jnp.einsum(
        "pcrj,rjx->rpcx", gathered, tables, preferred_element_type=jnp.float32
    ).reshape(band_rows, pieces, keep, 2, M)
    spectra_re, spectra_im = spectra[:, :, :, 0], spectra[:, :, :, 1]
    real_part = jnp.sum(
        phase_re[:, :, None, :] * spectra_re - phase_im[:, :, None, :] * spectra_im, axis=1
    )
    imag_part = jnp.sum(
        phase_re[:, :, None, :] * spectra_im + phase_im[:, :, None, :] * spectra_re, axis=1
    )
    fourier = jnp.stack([real_part, imag_part], axis=2)
    wavenumber = jnp.arange(M, dtype=jnp.int32)
    inverse = jnp.float32(1.0) / row_points.astype(jnp.float32)
    resolved = 2 * wavenumber[None, :] < row_points[:, None]
    fourier = jnp.where(
        resolved[:, None, None, :], fourier * inverse[:, None, None, None], jnp.float32(0.0)
    )
    fourier = fourier.astype(jnp.bfloat16)
    pick = (wave_order[None, :] == wavenumber[:, None]).astype(jnp.bfloat16)
    sorted_waves = jnp.einsum(
        "rctm,ms->sctr", fourier, pick, preferred_element_type=jnp.float32
    ).astype(jnp.bfloat16)
    count = lax.axis_size(LAT)
    sorted_waves = sorted_waves.reshape((count, slots) + sorted_waves.shape[1:])
    sorted_waves = lax.all_to_all(sorted_waves, LAT, split_axis=0, concat_axis=4, tiled=True)[0]
    my_slots = lax.dynamic_slice_in_dim(wave_order, lax.axis_index(LAT) * slots, slots)
    degree = jnp.arange(NDEG, dtype=jnp.int32)
    masked_table = jnp.where(
        degree[None, None, :] >= my_slots[:, None, None], legendre, jnp.zeros((), legendre.dtype)
    )
    result = jnp.einsum(
        "sctl,sln->sctn", sorted_waves, masked_table, preferred_element_type=jnp.float32
    )
    return result.astype(jnp.bfloat16)


def lat_split(mesh):
    count = mesh.shape["lat"]
    fast = len({tuple(getattr(d, "coords", (0,)))[0] for d in mesh.devices[:, 0]})
    if fast < 1 or count % fast != 0:
        fast = 1
    return count // fast, fast


def solution(mesh):
    outer, inner = lat_split(mesh)
    grid_mesh = jax.sharding.Mesh(
        mesh.devices.reshape(outer, inner, mesh.shape["lon"]), LAT + ("lon",)
    )
    return jax.shard_map(
        shards,
        mesh=grid_mesh,
        in_specs=(
            P(None, LAT, "lon"),
            P(None, LAT, "lon"),
            P(LAT, "lon"),
            P(LAT),
            P(),
            P(LAT, None, None),
        ),
        out_specs=P(LAT, "lon", None, None),
        check_vma=False,
    )
```

```python
import math

import jax
import jax.numpy as jnp
from jax import lax
from jax.sharding import PartitionSpec as P

M = 640
NDEG = 640
HALO = 3
SPLIT = 32
LAT = ("lat_outer", "lat_inner")


def extended(block, sides, width):
    for axis, dim in sides:
        count = lax.axis_size(axis)
        forward = [(i, i + 1) for i in range(count - 1)]
        backward = [(target, source) for source, target in forward]
        low = lax.ppermute(
            lax.slice_in_dim(block, block.shape[dim] - width, None, axis=dim), axis, forward
        )
        high = lax.ppermute(lax.slice_in_dim(block, 0, width, axis=dim), axis, backward)
        block = jnp.concatenate([low, block, high], axis=dim)
    return block


def turn_sincos(product, points):
    n = points.astype(jnp.float32)
    quarter = 4.0 * product.astype(jnp.float32)
    turn = jnp.floor(quarter * (1.0 / n) + 0.5)
    x = (quarter - turn * n) * (0.5 * math.pi / n)
    x2 = x * x
    sine = x * (1.0 + x2 * (-1.0 / 6 + x2 * (1.0 / 120 + x2 * (-1.0 / 5040 + x2 * (1.0 / 362880)))))
    cosine = 1.0 + x2 * (-0.5 + x2 * (1.0 / 24 + x2 * (-1.0 / 720 + x2 * (1.0 / 40320 - x2 * (1.0 / 3628800)))))
    quadrant = turn.astype(jnp.int32) & 3
    swap = (quadrant & 1) == 1
    cos_out = jnp.where(swap, sine, cosine)
    sin_out = jnp.where(swap, cosine, sine)
    cos_out = jnp.where((quadrant == 1) | (quadrant == 2), -cos_out, cos_out)
    sin_out = jnp.where(quadrant >= 2, -sin_out, sin_out)
    return cos_out, sin_out


def segment_tables(points, seg_len, waves):
    wavenumber = jnp.arange(waves, dtype=jnp.int32)
    high = jnp.arange(-(-seg_len // SPLIT), dtype=jnp.int32) * SPLIT
    low = jnp.arange(SPLIT, dtype=jnp.int32)
    rows = points[:, None, None]
    ch, sh = turn_sincos(high[None, :, None] * wavenumber[None, None, :], rows)
    cl, sl = turn_sincos(low[None, :, None] * wavenumber[None, None, :], rows)
    ch, sh = ch[:, :, None, :], sh[:, :, None, :]
    cl, sl = cl[:, None, :, :], sl[:, None, :, :]
    cosine = ch * cl - sh * sl
    sine = sh * cl + ch * sl
    table = jnp.concatenate([cosine, -sine], axis=3).astype(jnp.bfloat16)
    return table.reshape(points.shape[0], -1, 2 * waves)[:, :seg_len]


def phase_pair(points, starts, waves):
    wavenumber = jnp.arange(waves, dtype=jnp.int32)
    cosine, sine = turn_sincos(starts[None, :, None] * wavenumber[None, None, :], points[:, None, None])
    return (cosine, -sine)


def shards(grid, cubic_weights, dep_base, row_points, wave_order, legendre):
    columns, band_rows, seg_len = grid.shape
    pieces = lax.axis_size("lon")
    keep = columns // pieces
    slots = legendre.shape[0]
    first_row = lax.axis_index(LAT) * band_rows
    first_point = lax.axis_index("lon") * seg_len
    padded = extended(grid, ((LAT, 1),), HALO)
    offset = dep_base - (first_row + jnp.arange(band_rows, dtype=jnp.int32))[:, None]
    arrival = jnp.zeros((columns, band_rows, seg_len), jnp.float32)
    for displace in range(-HALO, HALO + 1):
        stencil = jnp.zeros((band_rows, seg_len), jnp.float32)
        for node in range(4):
            stencil = stencil + jnp.where(
                offset - 1 + node == displace, cubic_weights[node], jnp.float32(0.0)
            )
        arrival = arrival + stencil[None] * padded[
            :, HALO + displace : HALO + displace + band_rows, :
        ].astype(jnp.float32)
    inside = (first_point + jnp.arange(seg_len, dtype=jnp.int32))[None, :] < row_points[:, None]
    arrival = jnp.where(inside[None], arrival, jnp.float32(0.0)).astype(jnp.bfloat16)
    gathered = lax.all_to_all(
        arrival.reshape(pieces, keep, band_rows, seg_len), "lon", split_axis=0, concat_axis=0, tiled=True
    )
    tables = segment_tables(row_points, seg_len, M)
    starts = jnp.arange(pieces, dtype=jnp.int32) * seg_len
    phase_re, phase_im = phase_pair(row_points, starts, M)
    spectra = jnp.einsum(
        "pcrj,rjx->rpcx", gathered, tables, preferred_element_type=jnp.float32
    )
    spectra_re, spectra_im = spectra[..., :M], spectra[..., M:]
    real_part = jnp.sum(
        phase_re[:, :, None, :] * spectra_re - phase_im[:, :, None, :] * spectra_im, axis=1
    )
    imag_part = jnp.sum(
        phase_re[:, :, None, :] * spectra_im + phase_im[:, :, None, :] * spectra_re, axis=1
    )
    fourier = jnp.stack([real_part, imag_part], axis=2)
    wavenumber = jnp.arange(M, dtype=jnp.int32)
    inverse = jnp.float32(1.0) / row_points.astype(jnp.float32)
    resolved = 2 * wavenumber[None, :] < row_points[:, None]
    fourier = jnp.where(
        resolved[:, None, None, :], fourier * inverse[:, None, None, None], jnp.float32(0.0)
    )
    fourier = fourier.astype(jnp.bfloat16)
    pick = (wave_order[None, :] == wavenumber[:, None]).astype(jnp.bfloat16)
    sorted_waves = jnp.einsum(
        "rctm,ms->sctr", fourier, pick, preferred_element_type=jnp.float32
    ).astype(jnp.bfloat16)
    count = lax.axis_size(LAT)
    sorted_waves = sorted_waves.reshape((count, slots) + sorted_waves.shape[1:])
    sorted_waves = lax.all_to_all(sorted_waves, LAT, split_axis=0, concat_axis=4, tiled=True)[0]
    my_slots = lax.dynamic_slice_in_dim(wave_order, lax.axis_index(LAT) * slots, slots)
    degree = jnp.arange(NDEG, dtype=jnp.int32)
    masked_table = jnp.where(
        degree[None, None, :] >= my_slots[:, None, None], legendre, jnp.zeros((), legendre.dtype)
    )
    result = jnp.einsum(
        "sctl,sln->sctn", sorted_waves, masked_table, preferred_element_type=jnp.float32
    )
    return result.astype(jnp.bfloat16)


def lat_split(mesh):
    count = mesh.shape["lat"]
    fast = len({tuple(getattr(d, "coords", (0,)))[0] for d in mesh.devices[:, 0]})
    if fast < 1 or count % fast != 0:
        fast = 1
    return count // fast, fast


def solution(mesh):
    outer, inner = lat_split(mesh)
    grid_mesh = jax.sharding.Mesh(
        mesh.devices.reshape(outer, inner, mesh.shape["lon"]), LAT + ("lon",)
    )
    return jax.shard_map(
        shards,
        mesh=grid_mesh,
        in_specs=(
            P(None, LAT, "lon"),
            P(None, LAT, "lon"),
            P(LAT, "lon"),
            P(LAT),
            P(),
            P(LAT, None, None),
        ),
        out_specs=P(LAT, "lon", None, None),
        check_vma=False,
    )
```

```python
import math

import jax
import jax.numpy as jnp
from jax import lax
from jax.sharding import PartitionSpec as P

M = 640
NDEG = 640
HALO = 3
SPLIT = 32
LAT = ("lat_outer", "lat_inner")


def extended(block, sides, width):
    for axis, dim in sides:
        count = lax.axis_size(axis)
        forward = [(i, i + 1) for i in range(count - 1)]
        backward = [(target, source) for source, target in forward]
        low = lax.ppermute(
            lax.slice_in_dim(block, block.shape[dim] - width, None, axis=dim), axis, forward
        )
        high = lax.ppermute(lax.slice_in_dim(block, 0, width, axis=dim), axis, backward)
        block = jnp.concatenate([low, block, high], axis=dim)
    return block


def turn_sincos(product, points):
    n = points.astype(jnp.float32)
    quarter = 4.0 * product.astype(jnp.float32)
    turn = jnp.floor(quarter * (1.0 / n) + 0.5)
    x = (quarter - turn * n) * (0.5 * math.pi / n)
    x2 = x * x
    sine = x * (1.0 + x2 * (-1.0 / 6 + x2 * (1.0 / 120 + x2 * (-1.0 / 5040 + x2 * (1.0 / 362880)))))
    cosine = 1.0 + x2 * (-0.5 + x2 * (1.0 / 24 + x2 * (-1.0 / 720 + x2 * (1.0 / 40320 - x2 * (1.0 / 3628800)))))
    quadrant = turn.astype(jnp.int32) & 3
    swap = (quadrant & 1) == 1
    cos_out = jnp.where(swap, sine, cosine)
    sin_out = jnp.where(swap, cosine, sine)
    cos_out = jnp.where((quadrant == 1) | (quadrant == 2), -cos_out, cos_out)
    sin_out = jnp.where(quadrant >= 2, -sin_out, sin_out)
    return cos_out, sin_out


def segment_tables(points, seg_len, waves):
    wavenumber = jnp.arange(waves, dtype=jnp.int32)
    high = jnp.arange(-(-seg_len // SPLIT), dtype=jnp.int32) * SPLIT
    low = jnp.arange(SPLIT, dtype=jnp.int32)
    rows = points[:, None, None]
    ch, sh = turn_sincos(high[None, :, None] * wavenumber[None, None, :], rows)
    cl, sl = turn_sincos(low[None, :, None] * wavenumber[None, None, :], rows)
    ch, sh = ch[:, :, None, :], sh[:, :, None, :]
    cl, sl = cl[:, None, :, :], sl[:, None, :, :]
    cosine = ch * cl - sh * sl
    sine = sh * cl + ch * sl
    table = jnp.concatenate([cosine, -sine], axis=3).astype(jnp.bfloat16)
    return table.reshape(points.shape[0], -1, 2 * waves)[:, :seg_len]


def phase_pair(points, starts, waves):
    wavenumber = jnp.arange(waves, dtype=jnp.int32)
    cosine, sine = turn_sincos(starts[None, :, None] * wavenumber[None, None, :], points[:, None, None])
    return (cosine, -sine)


def shards(grid, cubic_weights, dep_base, row_points, wave_order, legendre):
    columns, band_rows, seg_len = grid.shape
    pieces = lax.axis_size("lon")
    keep = columns // pieces
    slots = legendre.shape[0]
    first_row = lax.axis_index(LAT) * band_rows
    first_point = lax.axis_index("lon") * seg_len
    padded = extended(grid, ((LAT, 1),), HALO)
    offset = dep_base - (first_row + jnp.arange(band_rows, dtype=jnp.int32))[:, None]
    arrival = jnp.zeros((columns, band_rows, seg_len), jnp.float32)
    for displace in range(-HALO, HALO + 1):
        stencil = jnp.zeros((band_rows, seg_len), jnp.float32)
        for node in range(4):
            stencil = stencil + jnp.where(
                offset - 1 + node == displace, cubic_weights[node], jnp.float32(0.0)
            )
        arrival = arrival + stencil[None] * padded[
            :, HALO + displace : HALO + displace + band_rows, :
        ].astype(jnp.float32)
    inside = (first_point + jnp.arange(seg_len, dtype=jnp.int32))[None, :] < row_points[:, None]
    arrival = jnp.where(inside[None], arrival, jnp.float32(0.0)).astype(jnp.bfloat16)
    gathered = lax.all_to_all(
        arrival.reshape(pieces, keep, band_rows, seg_len), "lon", split_axis=0, concat_axis=0, tiled=True
    )
    tables = segment_tables(row_points, seg_len, M)
    starts = jnp.arange(pieces, dtype=jnp.int32) * seg_len
    phase_re, phase_im = phase_pair(row_points, starts, M)
    spectra = jnp.einsum(
        "pcrj,rjx->rpcx", gathered, tables, preferred_element_type=jnp.float32
    )
    spectra_re, spectra_im = spectra[..., :M], spectra[..., M:]
    real_part = jnp.sum(
        phase_re[:, :, None, :] * spectra_re - phase_im[:, :, None, :] * spectra_im, axis=1
    )
    imag_part = jnp.sum(
        phase_re[:, :, None, :] * spectra_im + phase_im[:, :, None, :] * spectra_re, axis=1
    )
    fourier = jnp.stack([real_part, imag_part], axis=2)
    wavenumber = jnp.arange(M, dtype=jnp.int32)
    inverse = jnp.float32(1.0) / row_points.astype(jnp.float32)
    resolved = 2 * wavenumber[None, :] < row_points[:, None]
    fourier = jnp.where(
        resolved[:, None, None, :], fourier * inverse[:, None, None, None], jnp.float32(0.0)
    )
    fourier = fourier.astype(jnp.bfloat16)
    count = lax.axis_size(LAT)
    pick = (wave_order[None, :] == wavenumber[:, None]).astype(jnp.bfloat16).reshape(M, count, slots)
    sorted_waves = jnp.einsum(
        "rctm,mqs->qsctr", fourier, pick, preferred_element_type=jnp.float32
    ).astype(jnp.bfloat16)
    sorted_waves = lax.all_to_all(sorted_waves, LAT, split_axis=0, concat_axis=4, tiled=True)[0]
    my_slots = lax.dynamic_slice_in_dim(wave_order, lax.axis_index(LAT) * slots, slots)
    degree = jnp.arange(NDEG, dtype=jnp.int32)
    masked_table = jnp.where(
        degree[None, None, :] >= my_slots[:, None, None], legendre, jnp.zeros((), legendre.dtype)
    )
    result = jnp.einsum(
        "sctl,sln->sctn", sorted_waves, masked_table, preferred_element_type=jnp.float32
    )
    return result.astype(jnp.bfloat16)


def lat_split(mesh):
    count = mesh.shape["lat"]
    fast = len({tuple(getattr(d, "coords", (0,)))[0] for d in mesh.devices[:, 0]})
    if fast < 1 or count % fast != 0:
        fast = 1
    return count // fast, fast


def solution(mesh):
    outer, inner = lat_split(mesh)
    grid_mesh = jax.sharding.Mesh(
        mesh.devices.reshape(outer, inner, mesh.shape["lon"]), LAT + ("lon",)
    )
    return jax.shard_map(
        shards,
        mesh=grid_mesh,
        in_specs=(
            P(None, LAT, "lon"),
            P(None, LAT, "lon"),
            P(LAT, "lon"),
            P(LAT),
            P(),
            P(LAT, None, None),
        ),
        out_specs=P(LAT, "lon", None, None),
        check_vma=False,
    )
```

```python
import math

import jax
import jax.numpy as jnp
from jax import lax
from jax.sharding import PartitionSpec as P

M = 640
NDEG = 640
HALO = 3
SPLIT = 32
LAT = ("lat_outer", "lat_inner")


def extended(block, sides, width):
    for axis, dim in sides:
        count = lax.axis_size(axis)
        forward = [(i, i + 1) for i in range(count - 1)]
        backward = [(target, source) for source, target in forward]
        low = lax.ppermute(block, axis, forward)
        high = lax.ppermute(block, axis, backward)
        size = block.shape[dim]
        block = jnp.concatenate(
            [lax.slice_in_dim(low, size - width, None, axis=dim), block, lax.slice_in_dim(high, 0, width, axis=dim)],
            axis=dim,
        )
    return block


def turn_sincos(product, points):
    n = points.astype(jnp.float32)
    quarter = 4.0 * product.astype(jnp.float32)
    turn = jnp.floor(quarter * (1.0 / n) + 0.5)
    x = (quarter - turn * n) * (0.5 * math.pi / n)
    x2 = x * x
    sine = x * (1.0 + x2 * (-1.0 / 6 + x2 * (1.0 / 120 + x2 * (-1.0 / 5040 + x2 * (1.0 / 362880)))))
    cosine = 1.0 + x2 * (-0.5 + x2 * (1.0 / 24 + x2 * (-1.0 / 720 + x2 * (1.0 / 40320 - x2 * (1.0 / 3628800)))))
    quadrant = turn.astype(jnp.int32) & 3
    swap = (quadrant & 1) == 1
    cos_out = jnp.where(swap, sine, cosine)
    sin_out = jnp.where(swap, cosine, sine)
    cos_out = jnp.where((quadrant == 1) | (quadrant == 2), -cos_out, cos_out)
    sin_out = jnp.where(quadrant >= 2, -sin_out, sin_out)
    return cos_out, sin_out


def segment_tables(points, seg_len, waves):
    wavenumber = jnp.arange(waves, dtype=jnp.int32)
    high = jnp.arange(-(-seg_len // SPLIT), dtype=jnp.int32) * SPLIT
    low = jnp.arange(SPLIT, dtype=jnp.int32)
    rows = points[:, None, None]
    ch, sh = turn_sincos(high[None, :, None] * wavenumber[None, None, :], rows)
    cl, sl = turn_sincos(low[None, :, None] * wavenumber[None, None, :], rows)
    ch, sh = ch[:, :, None, :], sh[:, :, None, :]
    cl, sl = cl[:, None, :, :], sl[:, None, :, :]
    cosine = ch * cl - sh * sl
    sine = sh * cl + ch * sl
    table = jnp.concatenate([cosine, -sine], axis=3).astype(jnp.bfloat16)
    return table.reshape(points.shape[0], -1, 2 * waves)[:, :seg_len]


def phase_pair(points, starts, waves):
    wavenumber = jnp.arange(waves, dtype=jnp.int32)
    cosine, sine = turn_sincos(starts[None, :, None] * wavenumber[None, None, :], points[:, None, None])
    return (cosine, -sine)


def shards(grid, cubic_weights, dep_base, row_points, wave_order, legendre):
    columns, band_rows, seg_len = grid.shape
    pieces = lax.axis_size("lon")
    keep = columns // pieces
    slots = legendre.shape[0]
    first_row = lax.axis_index(LAT) * band_rows
    first_point = lax.axis_index("lon") * seg_len
    padded = extended(grid, ((LAT, 1),), HALO)
    offset = dep_base - (first_row + jnp.arange(band_rows, dtype=jnp.int32))[:, None]
    arrival = jnp.zeros((columns, band_rows, seg_len), jnp.float32)
    for displace in range(-HALO, HALO + 1):
        stencil = jnp.zeros((band_rows, seg_len), jnp.float32)
        for node in range(4):
            stencil = stencil + jnp.where(
                offset - 1 + node == displace, cubic_weights[node], jnp.float32(0.0)
            )
        arrival = arrival + stencil[None] * padded[
            :, HALO + displace : HALO + displace + band_rows, :
        ].astype(jnp.float32)
    inside = (first_point + jnp.arange(seg_len, dtype=jnp.int32))[None, :] < row_points[:, None]
    arrival = jnp.where(inside[None], arrival, jnp.float32(0.0)).astype(jnp.bfloat16)
    gathered = lax.all_to_all(
        arrival.reshape(pieces, keep, band_rows, seg_len), "lon", split_axis=0, concat_axis=0, tiled=True
    )
    tables = segment_tables(row_points, seg_len, M)
    starts = jnp.arange(pieces, dtype=jnp.int32) * seg_len
    phase_re, phase_im = phase_pair(row_points, starts, M)
    spectra = jnp.einsum(
        "pcrj,rjx->rpcx", gathered, tables, preferred_element_type=jnp.float32
    )
    spectra_re, spectra_im = spectra[..., :M], spectra[..., M:]
    real_part = jnp.sum(
        phase_re[:, :, None, :] * spectra_re - phase_im[:, :, None, :] * spectra_im, axis=1
    )
    imag_part = jnp.sum(
        phase_re[:, :, None, :] * spectra_im + phase_im[:, :, None, :] * spectra_re, axis=1
    )
    fourier = jnp.stack([real_part, imag_part], axis=2)
    wavenumber = jnp.arange(M, dtype=jnp.int32)
    inverse = jnp.float32(1.0) / row_points.astype(jnp.float32)
    resolved = 2 * wavenumber[None, :] < row_points[:, None]
    fourier = jnp.where(
        resolved[:, None, None, :], fourier * inverse[:, None, None, None], jnp.float32(0.0)
    )
    fourier = fourier.astype(jnp.bfloat16)
    count = lax.axis_size(LAT)
    pick = (wave_order[None, :] == wavenumber[:, None]).astype(jnp.bfloat16).reshape(M, count, slots)
    sorted_waves = jnp.einsum(
        "rctm,mqs->qsctr", fourier, pick, preferred_element_type=jnp.float32
    ).astype(jnp.bfloat16)
    sorted_waves = lax.all_to_all(sorted_waves, LAT, split_axis=0, concat_axis=4, tiled=True)[0]
    my_slots = lax.dynamic_slice_in_dim(wave_order, lax.axis_index(LAT) * slots, slots)
    degree = jnp.arange(NDEG, dtype=jnp.int32)
    masked_table = jnp.where(
        degree[None, None, :] >= my_slots[:, None, None], legendre, jnp.zeros((), legendre.dtype)
    )
    result = jnp.einsum(
        "sctl,sln->sctn", sorted_waves, masked_table, preferred_element_type=jnp.float32
    )
    return result.astype(jnp.bfloat16)


def lat_split(mesh):
    count = mesh.shape["lat"]
    fast = len({tuple(getattr(d, "coords", (0,)))[0] for d in mesh.devices[:, 0]})
    if fast < 1 or count % fast != 0:
        fast = 1
    return count // fast, fast


def solution(mesh):
    outer, inner = lat_split(mesh)
    grid_mesh = jax.sharding.Mesh(
        mesh.devices.reshape(outer, inner, mesh.shape["lon"]), LAT + ("lon",)
    )
    return jax.shard_map(
        shards,
        mesh=grid_mesh,
        in_specs=(
            P(None, LAT, "lon"),
            P(None, LAT, "lon"),
            P(LAT, "lon"),
            P(LAT),
            P(),
            P(LAT, None, None),
        ),
        out_specs=P(LAT, "lon", None, None),
        check_vma=False,
    )
```

```python
import math

import jax
import jax.numpy as jnp
from jax import lax
from jax.sharding import PartitionSpec as P

M = 640
NDEG = 640
HALO = 3
SPLIT = 32
LAT = ("lat_outer", "lat_inner")


def extended(block, sides, width):
    for axis, dim in sides:
        count = lax.axis_size(axis)
        forward = [(i, i + 1) for i in range(count - 1)]
        backward = [(target, source) for source, target in forward]
        low = lax.ppermute(
            lax.slice_in_dim(block, block.shape[dim] - width, None, axis=dim), axis, forward
        )
        high = lax.ppermute(lax.slice_in_dim(block, 0, width, axis=dim), axis, backward)
        block = jnp.concatenate([low, block, high], axis=dim)
    return block


def turn_sincos(product, points):
    n = points.astype(jnp.float32)
    quarter = 4.0 * product.astype(jnp.float32)
    turn = jnp.floor(quarter * (1.0 / n) + 0.5)
    x = (quarter - turn * n) * (0.5 * math.pi / n)
    x2 = x * x
    sine = x * (1.0 + x2 * (-1.0 / 6 + x2 * (1.0 / 120 + x2 * (-1.0 / 5040 + x2 * (1.0 / 362880)))))
    cosine = 1.0 + x2 * (-0.5 + x2 * (1.0 / 24 + x2 * (-1.0 / 720 + x2 * (1.0 / 40320 - x2 * (1.0 / 3628800)))))
    quadrant = turn.astype(jnp.int32) & 3
    swap = (quadrant & 1) == 1
    cos_out = jnp.where(swap, sine, cosine)
    sin_out = jnp.where(swap, cosine, sine)
    cos_out = jnp.where((quadrant == 1) | (quadrant == 2), -cos_out, cos_out)
    sin_out = jnp.where(quadrant >= 2, -sin_out, sin_out)
    return cos_out, sin_out


def segment_tables(points, seg_len, waves):
    wavenumber = jnp.arange(waves, dtype=jnp.int32)
    high = jnp.arange(-(-seg_len // SPLIT), dtype=jnp.int32) * SPLIT
    low = jnp.arange(SPLIT, dtype=jnp.int32)
    rows = points[:, None, None]
    ch, sh = turn_sincos(high[None, :, None] * wavenumber[None, None, :], rows)
    cl, sl = turn_sincos(low[None, :, None] * wavenumber[None, None, :], rows)
    ch, sh = ch[:, :, None, :], sh[:, :, None, :]
    cl, sl = cl[:, None, :, :], sl[:, None, :, :]
    cosine = ch * cl - sh * sl
    sine = sh * cl + ch * sl
    table = jnp.concatenate([cosine, -sine], axis=3).astype(jnp.bfloat16)
    return table.reshape(points.shape[0], -1, 2 * waves)[:, :seg_len]


def phase_pair(points, starts, waves):
    wavenumber = jnp.arange(waves, dtype=jnp.int32)
    cosine, sine = turn_sincos(starts[None, :, None] * wavenumber[None, None, :], points[:, None, None])
    return (cosine, -sine)


def shards(grid, cubic_weights, dep_base, row_points, wave_order, legendre):
    columns, band_rows, seg_len = grid.shape
    pieces = lax.axis_size("lon")
    keep = columns // pieces
    slots = legendre.shape[0]
    first_row = lax.axis_index(LAT) * band_rows
    first_point = lax.axis_index("lon") * seg_len
    padded = extended(grid, ((LAT, 1),), HALO)
    offset = dep_base - (first_row + jnp.arange(band_rows, dtype=jnp.int32))[:, None]
    arrival = jnp.zeros((columns, band_rows, seg_len), jnp.float32)
    for displace in range(-HALO, HALO + 1):
        stencil = jnp.zeros((band_rows, seg_len), jnp.float32)
        for node in range(4):
            stencil = stencil + jnp.where(
                offset - 1 + node == displace, cubic_weights[node], jnp.float32(0.0)
            )
        arrival = arrival + stencil[None] * padded[
            :, HALO + displace : HALO + displace + band_rows, :
        ].astype(jnp.float32)
    inside = (first_point + jnp.arange(seg_len, dtype=jnp.int32))[None, :] < row_points[:, None]
    arrival = jnp.where(inside[None], arrival, jnp.float32(0.0)).astype(jnp.bfloat16)
    gathered = lax.all_to_all(
        arrival.reshape(pieces, keep, band_rows, seg_len), "lon", split_axis=0, concat_axis=0, tiled=True
    )
    tables = segment_tables(row_points, seg_len, M)
    starts = jnp.arange(pieces, dtype=jnp.int32) * seg_len
    phase_re, phase_im = phase_pair(row_points, starts, M)
    spectra = jnp.einsum(
        "pcrj,rjx->rpcx", gathered, tables, preferred_element_type=jnp.float32
    )
    spectra_re, spectra_im = spectra[..., :M], spectra[..., M:]
    real_part = jnp.sum(
        phase_re[:, :, None, :] * spectra_re - phase_im[:, :, None, :] * spectra_im, axis=1
    )
    imag_part = jnp.sum(
        phase_re[:, :, None, :] * spectra_im + phase_im[:, :, None, :] * spectra_re, axis=1
    )
    fourier = jnp.stack([real_part, imag_part], axis=2)
    wavenumber = jnp.arange(M, dtype=jnp.int32)
    inverse = jnp.float32(1.0) / row_points.astype(jnp.float32)
    resolved = 2 * wavenumber[None, :] < row_points[:, None]
    fourier = jnp.where(
        resolved[:, None, None, :], fourier * inverse[:, None, None, None], jnp.float32(0.0)
    )
    fourier = fourier.astype(jnp.bfloat16)
    count = lax.axis_size(LAT)
    pick = (wave_order[None, :] == wavenumber[:, None]).astype(jnp.bfloat16).reshape(M, count, slots)
    sorted_waves = jnp.einsum(
        "rctm,mqs->qsctr", fourier, pick, preferred_element_type=jnp.float32
    ).astype(jnp.bfloat16)
    sorted_waves = lax.all_to_all(sorted_waves, LAT, split_axis=0, concat_axis=4, tiled=True)[0]
    my_slots = lax.dynamic_slice_in_dim(wave_order, lax.axis_index(LAT) * slots, slots)
    degree = jnp.arange(NDEG, dtype=jnp.int32)
    masked_table = jnp.where(
        degree[None, None, :] >= my_slots[:, None, None], legendre, jnp.zeros((), legendre.dtype)
    )
    masked_table = lax.optimization_barrier(masked_table)
    result = jnp.einsum(
        "sctl,sln->sctn", sorted_waves, masked_table, preferred_element_type=jnp.float32
    )
    return result.astype(jnp.bfloat16)


def lat_split(mesh):
    count = mesh.shape["lat"]
    fast = len({tuple(getattr(d, "coords", (0,)))[0] for d in mesh.devices[:, 0]})
    if fast < 1 or count % fast != 0:
        fast = 1
    return count // fast, fast


def solution(mesh):
    outer, inner = lat_split(mesh)
    grid_mesh = jax.sharding.Mesh(
        mesh.devices.reshape(outer, inner, mesh.shape["lon"]), LAT + ("lon",)
    )
    return jax.shard_map(
        shards,
        mesh=grid_mesh,
        in_specs=(
            P(None, LAT, "lon"),
            P(None, LAT, "lon"),
            P(LAT, "lon"),
            P(LAT),
            P(),
            P(LAT, None, None),
        ),
        out_specs=P(LAT, "lon", None, None),
        check_vma=False,
    )
```

```python
import math

import jax
import jax.numpy as jnp
from jax import lax
from jax.sharding import PartitionSpec as P

M = 640
NDEG = 640
HALO = 3
SPLIT = 32
LAT = ("lat_outer", "lat_inner")


def extended(block, sides, width):
    for axis, dim in sides:
        count = lax.axis_size(axis)
        forward = [(i, i + 1) for i in range(count - 1)]
        backward = [(target, source) for source, target in forward]
        low = lax.ppermute(
            lax.slice_in_dim(block, block.shape[dim] - width, None, axis=dim), axis, forward
        )
        high = lax.ppermute(lax.slice_in_dim(block, 0, width, axis=dim), axis, backward)
        block = jnp.concatenate([low, block, high], axis=dim)
    return block


def turn_sincos(product, points):
    n = points.astype(jnp.float32)
    quarter = 4.0 * product.astype(jnp.float32)
    turn = jnp.floor(quarter * (1.0 / n) + 0.5)
    x = (quarter - turn * n) * (0.5 * math.pi / n)
    x2 = x * x
    sine = x * (1.0 + x2 * (-1.0 / 6 + x2 * (1.0 / 120 + x2 * (-1.0 / 5040 + x2 * (1.0 / 362880)))))
    cosine = 1.0 + x2 * (-0.5 + x2 * (1.0 / 24 + x2 * (-1.0 / 720 + x2 * (1.0 / 40320 - x2 * (1.0 / 3628800)))))
    quadrant = turn.astype(jnp.int32) & 3
    swap = (quadrant & 1) == 1
    cos_out = jnp.where(swap, sine, cosine)
    sin_out = jnp.where(swap, cosine, sine)
    cos_out = jnp.where((quadrant == 1) | (quadrant == 2), -cos_out, cos_out)
    sin_out = jnp.where(quadrant >= 2, -sin_out, sin_out)
    return cos_out, sin_out


def segment_tables(points, seg_len, waves):
    wavenumber = jnp.arange(waves, dtype=jnp.int32)
    high = jnp.arange(-(-seg_len // SPLIT), dtype=jnp.int32) * SPLIT
    low = jnp.arange(SPLIT, dtype=jnp.int32)
    rows = points[:, None, None]
    ch, sh = turn_sincos(high[None, :, None] * wavenumber[None, None, :], rows)
    cl, sl = turn_sincos(low[None, :, None] * wavenumber[None, None, :], rows)
    ch, sh = ch[:, :, None, :], sh[:, :, None, :]
    cl, sl = cl[:, None, :, :], sl[:, None, :, :]
    cosine = ch * cl - sh * sl
    sine = sh * cl + ch * sl
    table = jnp.concatenate([cosine, -sine], axis=3).astype(jnp.bfloat16)
    return table.reshape(points.shape[0], -1, 2 * waves)[:, :seg_len]


def phase_pair(points, starts, waves):
    wavenumber = jnp.arange(waves, dtype=jnp.int32)
    cosine, sine = turn_sincos(starts[None, :, None] * wavenumber[None, None, :], points[:, None, None])
    return (cosine, -sine)


def shards(grid, cubic_weights, dep_base, row_points, wave_order, legendre):
    columns, band_rows, seg_len = grid.shape
    pieces = lax.axis_size("lon")
    keep = columns // pieces
    slots = legendre.shape[0]
    first_row = lax.axis_index(LAT) * band_rows
    first_point = lax.axis_index("lon") * seg_len
    padded = extended(grid, ((LAT, 1),), HALO)
    offset = dep_base - (first_row + jnp.arange(band_rows, dtype=jnp.int32))[:, None]
    arrival = jnp.zeros((columns, band_rows, seg_len), jnp.float32)
    for displace in range(-HALO, HALO + 1):
        stencil = jnp.zeros((band_rows, seg_len), jnp.float32)
        for node in range(4):
            stencil = stencil + jnp.where(
                offset - 1 + node == displace, cubic_weights[node], jnp.float32(0.0)
            )
        arrival = arrival + stencil[None] * padded[
            :, HALO + displace : HALO + displace + band_rows, :
        ].astype(jnp.float32)
    inside = (first_point + jnp.arange(seg_len, dtype=jnp.int32))[None, :] < row_points[:, None]
    arrival = jnp.where(inside[None], arrival, jnp.float32(0.0)).astype(jnp.bfloat16)
    gathered = lax.all_to_all(
        arrival.reshape(pieces, keep, band_rows, seg_len), "lon", split_axis=0, concat_axis=0, tiled=True
    )
    tables = segment_tables(row_points, seg_len, M)
    starts = jnp.arange(pieces, dtype=jnp.int32) * seg_len
    phase_re, phase_im = phase_pair(row_points, starts, M)
    spectra = jnp.einsum(
        "pcrj,rjx->rpcx", gathered, tables, preferred_element_type=jnp.float32
    )
    spectra_re, spectra_im = spectra[..., :M], spectra[..., M:]
    real_part = jnp.sum(
        phase_re[:, :, None, :] * spectra_re - phase_im[:, :, None, :] * spectra_im, axis=1
    )
    imag_part = jnp.sum(
        phase_re[:, :, None, :] * spectra_im + phase_im[:, :, None, :] * spectra_re, axis=1
    )
    fourier = jnp.stack([real_part, imag_part], axis=2)
    wavenumber = jnp.arange(M, dtype=jnp.int32)
    inverse = jnp.float32(1.0) / row_points.astype(jnp.float32)
    resolved = 2 * wavenumber[None, :] < row_points[:, None]
    fourier = jnp.where(
        resolved[:, None, None, :], fourier * inverse[:, None, None, None], jnp.float32(0.0)
    )
    fourier = fourier.astype(jnp.bfloat16)
    count = lax.axis_size(LAT)
    pick = (wave_order[None, :] == wavenumber[:, None]).astype(jnp.bfloat16).reshape(M, count, slots)
    sorted_waves = jnp.einsum(
        "rctm,mqs->qsctr", fourier, pick, preferred_element_type=jnp.float32
    ).astype(jnp.bfloat16)
    sorted_waves = lax.all_to_all(sorted_waves, LAT, split_axis=0, concat_axis=0, tiled=True)
    my_slots = lax.dynamic_slice_in_dim(wave_order, lax.axis_index(LAT) * slots, slots)
    degree = jnp.arange(NDEG, dtype=jnp.int32)
    table = legendre.reshape(slots, count, band_rows, NDEG)
    result = jnp.einsum(
        "qsctr,sqrn->sctn", sorted_waves, table, preferred_element_type=jnp.float32
    )
    result = jnp.where(degree[None, None, None, :] >= my_slots[:, None, None, None], result, jnp.float32(0.0))
    return result.astype(jnp.bfloat16)


def lat_split(mesh):
    count = mesh.shape["lat"]
    fast = len({tuple(getattr(d, "coords", (0,)))[0] for d in mesh.devices[:, 0]})
    if fast < 1 or count % fast != 0:
        fast = 1
    return count // fast, fast


def solution(mesh):
    outer, inner = lat_split(mesh)
    grid_mesh = jax.sharding.Mesh(
        mesh.devices.reshape(outer, inner, mesh.shape["lon"]), LAT + ("lon",)
    )
    return jax.shard_map(
        shards,
        mesh=grid_mesh,
        in_specs=(
            P(None, LAT, "lon"),
            P(None, LAT, "lon"),
            P(LAT, "lon"),
            P(LAT),
            P(),
            P(LAT, None, None),
        ),
        out_specs=P(LAT, "lon", None, None),
        check_vma=False,
    )
```

```python
import math

import jax
import jax.numpy as jnp
from jax import lax
from jax.sharding import PartitionSpec as P

M = 640
NDEG = 640
HALO = 3
SPLIT = 32
LAT = ("lat_outer", "lat_inner")


def extended(block, sides, width):
    for axis, dim in sides:
        count = lax.axis_size(axis)
        forward = [(i, i + 1) for i in range(count - 1)]
        backward = [(target, source) for source, target in forward]
        low = lax.ppermute(
            lax.slice_in_dim(block, block.shape[dim] - width, None, axis=dim), axis, forward
        )
        high = lax.ppermute(lax.slice_in_dim(block, 0, width, axis=dim), axis, backward)
        block = jnp.concatenate([low, block, high], axis=dim)
    return block


def turn_sincos(product, points):
    n = points.astype(jnp.float32)
    quarter = 4.0 * product.astype(jnp.float32)
    turn = jnp.floor(quarter * (1.0 / n) + 0.5)
    x = (quarter - turn * n) * (0.5 * math.pi / n)
    x2 = x * x
    sine = x * (1.0 + x2 * (-1.0 / 6 + x2 * (1.0 / 120 + x2 * (-1.0 / 5040 + x2 * (1.0 / 362880)))))
    cosine = 1.0 + x2 * (-0.5 + x2 * (1.0 / 24 + x2 * (-1.0 / 720 + x2 * (1.0 / 40320 - x2 * (1.0 / 3628800)))))
    quadrant = turn.astype(jnp.int32) & 3
    swap = (quadrant & 1) == 1
    cos_out = jnp.where(swap, sine, cosine)
    sin_out = jnp.where(swap, cosine, sine)
    cos_out = jnp.where((quadrant == 1) | (quadrant == 2), -cos_out, cos_out)
    sin_out = jnp.where(quadrant >= 2, -sin_out, sin_out)
    return cos_out, sin_out


def segment_tables(points, seg_len, waves):
    wavenumber = jnp.arange(waves, dtype=jnp.int32)
    high = jnp.arange(-(-seg_len // SPLIT), dtype=jnp.int32) * SPLIT
    low = jnp.arange(SPLIT, dtype=jnp.int32)
    rows = points[:, None, None]
    ch, sh = turn_sincos(high[None, :, None] * wavenumber[None, None, :], rows)
    cl, sl = turn_sincos(low[None, :, None] * wavenumber[None, None, :], rows)
    ch, sh = ch[:, :, None, :], sh[:, :, None, :]
    cl, sl = cl[:, None, :, :], sl[:, None, :, :]
    cosine = ch * cl - sh * sl
    sine = sh * cl + ch * sl
    table = jnp.concatenate([cosine, -sine], axis=3).astype(jnp.bfloat16)
    return table.reshape(points.shape[0], -1, 2 * waves)[:, :seg_len]


def phase_pair(points, starts, waves):
    wavenumber = jnp.arange(waves, dtype=jnp.int32)
    cosine, sine = turn_sincos(starts[None, :, None] * wavenumber[None, None, :], points[:, None, None])
    return (cosine, -sine)


def shards(grid, cubic_weights, dep_base, row_points, wave_order, legendre):
    columns, band_rows, seg_len = grid.shape
    pieces = lax.axis_size("lon")
    keep = columns // pieces
    slots = legendre.shape[0]
    first_row = lax.axis_index(LAT) * band_rows
    first_point = lax.axis_index("lon") * seg_len
    padded = extended(grid, ((LAT, 1),), HALO)
    offset = dep_base - (first_row + jnp.arange(band_rows, dtype=jnp.int32))[:, None]
    arrival = jnp.zeros((columns, band_rows, seg_len), jnp.float32)
    for displace in range(-HALO, HALO + 1):
        stencil = jnp.zeros((band_rows, seg_len), jnp.float32)
        for node in range(4):
            stencil = stencil + jnp.where(
                offset - 1 + node == displace, cubic_weights[node], jnp.float32(0.0)
            )
        arrival = arrival + stencil[None] * padded[
            :, HALO + displace : HALO + displace + band_rows, :
        ].astype(jnp.float32)
    inside = (first_point + jnp.arange(seg_len, dtype=jnp.int32))[None, :] < row_points[:, None]
    arrival = jnp.where(inside[None], arrival, jnp.float32(0.0)).astype(jnp.bfloat16)
    gathered = lax.all_to_all(
        arrival.reshape(pieces, keep, band_rows, seg_len), "lon", split_axis=0, concat_axis=0, tiled=True
    )
    tables = segment_tables(row_points, seg_len, M)
    starts = jnp.arange(pieces, dtype=jnp.int32) * seg_len
    phase_re, phase_im = phase_pair(row_points, starts, M)
    wavenumber = jnp.arange(M, dtype=jnp.int32)
    inverse = jnp.float32(1.0) / row_points.astype(jnp.float32)
    resolved = 2 * wavenumber[None, :] < row_points[:, None]
    scale = jnp.where(resolved, inverse[:, None], jnp.float32(0.0))[:, None, :]
    phase_re, phase_im = phase_re * scale, phase_im * scale
    spectra = jnp.einsum(
        "pcrj,rjx->rpcx", gathered, tables, preferred_element_type=jnp.float32
    )
    spectra_re, spectra_im = spectra[..., :M], spectra[..., M:]
    real_part = jnp.sum(
        phase_re[:, :, None, :] * spectra_re - phase_im[:, :, None, :] * spectra_im, axis=1
    )
    imag_part = jnp.sum(
        phase_re[:, :, None, :] * spectra_im + phase_im[:, :, None, :] * spectra_re, axis=1
    )
    fourier = jnp.stack([real_part, imag_part], axis=2).astype(jnp.bfloat16)
    count = lax.axis_size(LAT)
    pick = (wave_order[None, :] == wavenumber[:, None]).astype(jnp.bfloat16).reshape(M, count, slots)
    sorted_waves = jnp.einsum(
        "rctm,mqs->qsctr", fourier, pick, preferred_element_type=jnp.float32
    ).astype(jnp.bfloat16)
    sorted_waves = lax.all_to_all(sorted_waves, LAT, split_axis=0, concat_axis=4, tiled=True)[0]
    my_slots = lax.dynamic_slice_in_dim(wave_order, lax.axis_index(LAT) * slots, slots)
    degree = jnp.arange(NDEG, dtype=jnp.int32)
    masked_table = jnp.where(
        degree[None, None, :] >= my_slots[:, None, None], legendre, jnp.zeros((), legendre.dtype)
    )
    result = jnp.einsum(
        "sctl,sln->sctn", sorted_waves, masked_table, preferred_element_type=jnp.float32
    )
    return result.astype(jnp.bfloat16)


def lat_split(mesh):
    count = mesh.shape["lat"]
    fast = len({tuple(getattr(d, "coords", (0,)))[0] for d in mesh.devices[:, 0]})
    if fast < 1 or count % fast != 0:
        fast = 1
    return count // fast, fast


def solution(mesh):
    outer, inner = lat_split(mesh)
    grid_mesh = jax.sharding.Mesh(
        mesh.devices.reshape(outer, inner, mesh.shape["lon"]), LAT + ("lon",)
    )
    return jax.shard_map(
        shards,
        mesh=grid_mesh,
        in_specs=(
            P(None, LAT, "lon"),
            P(None, LAT, "lon"),
            P(LAT, "lon"),
            P(LAT),
            P(),
            P(LAT, None, None),
        ),
        out_specs=P(LAT, "lon", None, None),
        check_vma=False,
    )
```
